256 devices in a mesh: gx: 8 (over z), gy: 8 (over x, core), vec: 4 (over y).
Axes of the slice: x: 4, y: 4, z: 8, core: 2. Of those that a mesh axis runs over, the one named last changes fastest.
Arguments:
- tangents: float32 [128, 256, 2, 512], P('gx', 'gy', None, 'vec'), may hold values from -120 to 120
- base_flow: float32 [128, 256, 3], P('gx', 'gy'), may hold values from -1.5 to 1.5
Outputs:
- rotated: float32 [128, 256, 2, 512], P('gx', 'gy', None, 'vec')
The draws below stay inside these ranges and needn't reach their ends.
All inputs are finite; a program needn't handle non-finite values.
Results may differ from the reference program's by a relative error of at most 0.00027.
Values sent between devices are 32-bit elements; how exact they have to be, the bound alone decides.
No kernel may reach another device: no remote copies, remote signals or barrier semaphores. Data moves between devices by JAX's collectives and lax.ppermute only.
A program may use at most 64 MiB of HBM per device.

```python
import math
import jax
import jax.numpy as jnp
from jax import lax

M = 512
NS_ITERS = 4
NX = 128
NY = 256


def draw_tangents(key, part):
    subkeys = jax.random.split(key, 3)
    normal_draw = jax.random.normal(subkeys[0], (NX, NY, 2, M), jnp.float32)
    mixing = jax.random.normal(subkeys[1], (M, M), jnp.float32) * (0.6 / math.sqrt(M))
    mixed_draw = normal_draw + jnp.dot(normal_draw.reshape(-1, M), mixing, precision=lax.Precision.HIGHEST).reshape(normal_draw.shape)
    scales = jnp.exp(jax.random.uniform(subkeys[2], (M,), jnp.float32) * math.log(10.0))
    drawn = mixed_draw * scales
    return jnp.clip(drawn, -120.0, 120.0)


def level_of(rng, extent, pieces, smallest, top_value):
    def one(axis_at, blocks):
        draws = jax.random.uniform(jax.random.fold_in(jax.random.fold_in(rng, 6), axis_at), (blocks,), jnp.float32, smallest / len(pieces), top_value / len(pieces))
        return jnp.repeat(jnp.exp(draws), extent[axis_at] // blocks).reshape((-1,) + (1,) * (len(extent) - axis_at - 1))

    factor_of = one(*pieces[0])
    for cut in pieces[1:]:
        factor_of = factor_of * one(*cut)
    return factor_of


def setup_inputs(seed: int = 0) -> dict:
    key_of = jax.random.split(jax.random.key(seed), 3)
    tangents = draw_tangents(jax.random.fold_in(key_of[2], 71), 0)
    base_flow = jnp.clip(jax.random.uniform(key_of[1], (NX, NY, 3), jnp.float32, -1.5, 1.5) * level_of(key_of[1], (NX, NY, 3), ((0, 8), (1, 8)), -0.4, 0.0), -1.5, 1.5)
    return dict(tangents=tangents, base_flow=base_flow)


time_step = 0.25
viscous = 0.05
spreading_share = 0.05
buoyancy = 1.0

def tendency(padded, flow):
    middle_node = padded[2:-2, 2:-2]
    east_two = padded[4:, 2:-2]
    east_one = padded[3:-1, 2:-2]
    west_one = padded[1:-3, 2:-2]
    west_two = padded[:-4, 2:-2]
    north_two = padded[2:-2, 4:]
    north_one = padded[2:-2, 3:-1]
    south_one = padded[2:-2, 1:-3]
    south_two = padded[2:-2, :-4]
    deriv_x = (8.0 * (east_one - west_one) - (east_two - west_two)) / 12.0
    deriv_y = (8.0 * (north_one - south_one) - (north_two - south_two)) / 12.0
    second_derivative_sum = (16.0 * (east_one + west_one + north_one + south_one) - (east_two + west_two + north_two + south_two) - 60.0 * middle_node) / 12.0
    vel_x = flow[:, :, 0][:, :, None, None]
    vel_y = flow[:, :, 1][:, :, None, None]
    thermal_forcing = flow[:, :, 2][:, :, None]
    transport_share = -(vel_x * deriv_x + vel_y * deriv_y)
    swirl_profile = transport_share[:, :, 0] + viscous * second_derivative_sum[:, :, 0] + buoyancy * deriv_x[:, :, 1]
    heat_profile = transport_share[:, :, 1] + spreading_share * second_derivative_sum[:, :, 1] + thermal_forcing * middle_node[:, :, 0]
    return jnp.stack([swirl_profile, heat_profile], axis=2)

def combine_sections(field, slope_one, slope_two, slope_three, slope_four):
    return field + time_step / 6.0 * (slope_one + 2.0 * slope_two + 2.0 * slope_three + slope_four)

def extend(field):
    wrapped = jnp.concatenate([field[-2:], field, field[:2]], axis=0)
    return jnp.pad(wrapped, ((0, 0), (2, 2), (0, 0), (0, 0)))

def runge_kutta(field, flow):
    slope_one = tendency(extend(field), flow)
    slope_two = tendency(extend(field + 0.5 * time_step * slope_one), flow)
    slope_three = tendency(extend(field + 0.5 * time_step * slope_two), flow)
    slope_four = tendency(extend(field + time_step * slope_three), flow)
    return combine_sections(field, slope_one, slope_two, slope_three, slope_four)

def inverse_root(gram_matrix):
    highest = lax.Precision.HIGHEST
    scale_norm = jnp.sqrt(jnp.sum(gram_matrix * gram_matrix) + 1e-06)
    identity = jnp.eye(gram_matrix.shape[0], dtype=jnp.float32)
    iterate_y = gram_matrix / scale_norm
    iterate_z = identity
    for iteration in range(NS_ITERS):
        poly = 1.5 * identity - 0.5 * jnp.dot(iterate_z, iterate_y, precision=highest, preferred_element_type=jnp.float32)
        iterate_y = jnp.dot(iterate_y, poly, precision=highest, preferred_element_type=jnp.float32)
        iterate_z = jnp.dot(poly, iterate_z, precision=highest, preferred_element_type=jnp.float32)
    return iterate_z / jnp.sqrt(scale_norm)

def reference(tangents, base_flow):
    highest = lax.Precision.HIGHEST
    block_width = 64 if M % 64 == 0 else M
    blocks = tangents.reshape(NX, NY, 2, M // block_width, block_width).transpose(3, 0, 1, 2, 4)

    def advance(field):
        return runge_kutta(field, base_flow)
    advanced = lax.map(advance, blocks).transpose(1, 2, 3, 0, 4).reshape(NX, NY, 2, M)
    flat_rows = advanced.reshape(-1, M)
    gram_matrix = lax.dot_general(flat_rows, flat_rows, (((0,), (0,)), ((), ())), precision=highest, preferred_element_type=jnp.float32) / (NX * NY)
    root = inverse_root(gram_matrix)
    return jnp.dot(flat_rows, root, precision=highest, preferred_element_type=jnp.float32).reshape(NX, NY, 2, M)
```

```python
import jax
import jax.numpy as jnp
from jax import lax
from jax.sharding import PartitionSpec as P

NS_ITERS = 4


time_step = 0.25
viscous = 0.05
spreading_share = 0.05
buoyancy = 1.0


def with_halo(value, sides, width, wrap):
    for axis, dim in sides:
        size, length = (lax.axis_size(axis), value.shape[dim])
        up = [(i, (i + 1) % size) for i in range(size if wrap else size - 1)]
        down = [(j, i) for i, j in up]
        last = lax.slice_in_dim(value, length - width, length, axis=dim)
        leading = lax.slice_in_dim(value, 0, width, axis=dim)
        before = lax.ppermute(last, axis, up)
        after = lax.ppermute(leading, axis, down)
        value = jnp.concatenate([before, value, after], axis=dim)
    return value


def tendency(padded, flow):
    middle_node = padded[2:-2, 2:-2]
    east_two = padded[4:, 2:-2]
    east_one = padded[3:-1, 2:-2]
    west_one = padded[1:-3, 2:-2]
    west_two = padded[:-4, 2:-2]
    north_two = padded[2:-2, 4:]
    north_one = padded[2:-2, 3:-1]
    south_one = padded[2:-2, 1:-3]
    south_two = padded[2:-2, :-4]
    deriv_x = (8.0 * (east_one - west_one) - (east_two - west_two)) / 12.0
    deriv_y = (8.0 * (north_one - south_one) - (north_two - south_two)) / 12.0
    second_derivative_sum = (
        16.0 * (east_one + west_one + north_one + south_one)
        - (east_two + west_two + north_two + south_two)
        - 60.0 * middle_node
    ) / 12.0
    vel_x = flow[:, :, 0][:, :, None, None]
    vel_y = flow[:, :, 1][:, :, None, None]
    thermal_forcing = flow[:, :, 2][:, :, None]
    transport_share = -(vel_x * deriv_x + vel_y * deriv_y)
    swirl_profile = (
        transport_share[:, :, 0]
        + viscous * second_derivative_sum[:, :, 0]
        + buoyancy * deriv_x[:, :, 1]
    )
    heat_profile = (
        transport_share[:, :, 1]
        + spreading_share * second_derivative_sum[:, :, 1]
        + thermal_forcing * middle_node[:, :, 0]
    )
    return jnp.stack([swirl_profile, heat_profile], axis=2)


def combine_sections(field, slope_one, slope_two, slope_three, slope_four):
    return field + time_step / 6.0 * (slope_one + 2.0 * slope_two + 2.0 * slope_three + slope_four)


def add_rim(field, width):
    wider = with_halo(field, (("gx", 0),), width, True)
    return with_halo(wider, (("gy", 1),), width, False)


def inverse_root(gram_matrix):
    highest = lax.Precision.HIGHEST
    scale_norm = jnp.sqrt(jnp.sum(gram_matrix * gram_matrix) + 1e-06)
    identity = jnp.eye(gram_matrix.shape[0], dtype=jnp.float32)
    iterate_y = gram_matrix / scale_norm
    iterate_z = identity
    for iteration in range(NS_ITERS):
        poly = 1.5 * identity - 0.5 * jnp.dot(
            iterate_z, iterate_y, precision=highest, preferred_element_type=jnp.float32
        )
        iterate_y = jnp.dot(iterate_y, poly, precision=highest, preferred_element_type=jnp.float32)
        iterate_z = jnp.dot(poly, iterate_z, precision=highest, preferred_element_type=jnp.float32)
    return iterate_z / jnp.sqrt(scale_norm)


def reduce_order():
    steps = []
    for axis in ("gy", "vec", "gx"):
        size = lax.axis_size(axis)
        assert size & (size - 1) == 0
        bit = 1
        while bit < size:
            steps.append((axis, bit))
            bit *= 2
    return sorted(steps, key=lambda step: (step[1] if step[0] != "gy" else step[1] // 2, step[0] != "gy"))


def swap_perm(axis, bit):
    return [(i, i ^ bit) for i in range(lax.axis_size(axis))]


def tree_sum(value, order):
    halves = []
    for axis, bit in order:
        half = value.shape[0] // 2
        upper = (lax.axis_index(axis) // bit) % 2
        keep = lax.dynamic_slice_in_dim(value, upper * half, half, 0)
        send = lax.dynamic_slice_in_dim(value, (1 - upper) * half, half, 0)
        value = keep + lax.ppermute(send, axis, swap_perm(axis, bit))
        halves.append((axis, bit, upper))
    for axis, bit, upper in reversed(halves):
        other = lax.ppermute(value, axis, swap_perm(axis, bit))
        low = jnp.where(upper == 0, value, other)
        high = jnp.where(upper == 0, other, value)
        value = jnp.concatenate([low, high], 0)
    return value


def body(tangents, base_flow):
    highest = lax.Precision.HIGHEST
    slope_one = tendency(add_rim(tangents, 2), base_flow)
    slope_two = tendency(add_rim(tangents + 0.5 * time_step * slope_one, 2), base_flow)
    slope_three = tendency(add_rim(tangents + 0.5 * time_step * slope_two, 2), base_flow)
    slope_four = tendency(add_rim(tangents + time_step * slope_three, 2), base_flow)
    advanced = combine_sections(tangents, slope_one, slope_two, slope_three, slope_four)
    cells = tangents.shape[0] * lax.axis_size("gx") * tangents.shape[1] * lax.axis_size("gy")
    width_vec = advanced.shape[3]
    total_vec = width_vec * lax.axis_size("vec")
    points = lax.all_to_all(advanced, "vec", split_axis=0, concat_axis=3, tiled=True)
    flat_rows = points.reshape(-1, total_vec)
    partial_value = lax.dot_general(
        flat_rows,
        flat_rows,
        (((0,), (0,)), ((), ())),
        precision=highest,
        preferred_element_type=jnp.float32,
    )
    gram_matrix = tree_sum(partial_value, reduce_order()) / cells
    root = inverse_root(gram_matrix)
    turned = jnp.dot(
        flat_rows, root, precision=highest, preferred_element_type=jnp.float32
    ).reshape(points.shape)
    rotated = lax.all_to_all(turned, "vec", split_axis=3, concat_axis=0, tiled=True)
    return rotated


def solution(mesh):
    in_specs = (P("gx", "gy", None, "vec"), P("gx", "gy", None))
    out_specs = P("gx", "gy", None, "vec")
    return jax.shard_map(body, mesh=mesh, in_specs=in_specs, out_specs=out_specs, check_vma=False)
```

```python
import jax
import jax.numpy as jnp
from jax import lax
from jax.sharding import PartitionSpec as P

NS_ITERS = 4


time_step = 0.25
viscous = 0.05
spreading_share = 0.05
buoyancy = 1.0


def with_halo(value, sides, width, wrap):
    for axis, dim in sides:
        size, length = (lax.axis_size(axis), value.shape[dim])
        up = [(i, (i + 1) % size) for i in range(size if wrap else size - 1)]
        down = [(j, i) for i, j in up]
        last = lax.slice_in_dim(value, length - width, length, axis=dim)
        leading = lax.slice_in_dim(value, 0, width, axis=dim)
        before = lax.ppermute(last, axis, up)
        after = lax.ppermute(leading, axis, down)
        value = jnp.concatenate([before, value, after], axis=dim)
    return value


def tendency(padded, flow):
    middle_node = padded[2:-2, 2:-2]
    east_two = padded[4:, 2:-2]
    east_one = padded[3:-1, 2:-2]
    west_one = padded[1:-3, 2:-2]
    west_two = padded[:-4, 2:-2]
    north_two = padded[2:-2, 4:]
    north_one = padded[2:-2, 3:-1]
    south_one = padded[2:-2, 1:-3]
    south_two = padded[2:-2, :-4]
    deriv_x = (8.0 * (east_one - west_one) - (east_two - west_two)) / 12.0
    deriv_y = (8.0 * (north_one - south_one) - (north_two - south_two)) / 12.0
    second_derivative_sum = (
        16.0 * (east_one + west_one + north_one + south_one)
        - (east_two + west_two + north_two + south_two)
        - 60.0 * middle_node
    ) / 12.0
    vel_x = flow[:, :, 0][:, :, None, None]
    vel_y = flow[:, :, 1][:, :, None, None]
    thermal_forcing = flow[:, :, 2][:, :, None]
    transport_share = -(vel_x * deriv_x + vel_y * deriv_y)
    swirl_profile = (
        transport_share[:, :, 0]
        + viscous * second_derivative_sum[:, :, 0]
        + buoyancy * deriv_x[:, :, 1]
    )
    heat_profile = (
        transport_share[:, :, 1]
        + spreading_share * second_derivative_sum[:, :, 1]
        + thermal_forcing * middle_node[:, :, 0]
    )
    return jnp.stack([swirl_profile, heat_profile], axis=2)


def combine_sections(field, slope_one, slope_two, slope_three, slope_four):
    return field + time_step / 6.0 * (slope_one + 2.0 * slope_two + 2.0 * slope_three + slope_four)


def add_rim(field, width):
    wider = with_halo(field, (("gx", 0),), width, True)
    side = with_halo(field, (("gy", 1),), width, False)
    below = jnp.pad(side[:, :width], ((width, width),) + ((0, 0),) * (field.ndim - 1))
    above = jnp.pad(side[:, -width:], ((width, width),) + ((0, 0),) * (field.ndim - 1))
    return jnp.concatenate([below, wider, above], axis=1)


def inverse_root(gram_matrix):
    highest = lax.Precision.HIGHEST
    scale_norm = jnp.sqrt(jnp.sum(gram_matrix * gram_matrix) + 1e-06)
    identity = jnp.eye(gram_matrix.shape[0], dtype=jnp.float32)
    iterate_y = gram_matrix / scale_norm
    iterate_z = None
    for iteration in range(NS_ITERS):
        if iterate_z is None:
            product = iterate_y
        else:
            product = jnp.dot(iterate_z, iterate_y, precision=highest, preferred_element_type=jnp.float32)
        poly = 1.5 * identity - 0.5 * product
        if iteration + 1 < NS_ITERS:
            iterate_y = jnp.dot(iterate_y, poly, precision=highest, preferred_element_type=jnp.float32)
        if iterate_z is None:
            iterate_z = poly
        else:
            iterate_z = jnp.dot(poly, iterate_z, precision=highest, preferred_element_type=jnp.float32)
    return iterate_z / jnp.sqrt(scale_norm)


def reduce_groups():
    groups = []
    for axis in ("gy", "vec", "gx"):
        size = lax.axis_size(axis)
        assert size & (size - 1) == 0
        stride = 1
        if axis == "gy" and size > 1:
            groups.append((axis, 1, 2))
            stride = 2
        while stride < size:
            radix = 2 if axis == "gx" and stride == 1 and size > 4 else min(4, size // stride)
            groups.append((axis, stride, radix))
            stride *= radix
    first = [group for group in groups if group[0] == "gy"][:1]
    rest = [group for group in groups if group not in first]
    return first + sorted(rest, key=lambda group: group[1] if group[0] != "gy" else group[1] // 2)


def digit_perm(axis, stride, radix, offset):
    pairs = []
    for i in range(lax.axis_size(axis)):
        digit = (i // stride) % radix
        pairs.append((i, i + (((digit + offset) % radix) - digit) * stride))
    return pairs


def tree_sum(value, groups):
    done = []
    for axis, stride, radix in groups:
        piece = value.shape[0] // radix
        digit = (lax.axis_index(axis) // stride) % radix
        total = lax.dynamic_slice_in_dim(value, digit * piece, piece, 0)
        for offset in range(1, radix):
            send = lax.dynamic_slice_in_dim(value, ((digit + offset) % radix) * piece, piece, 0)
            total = total + lax.ppermute(send, axis, digit_perm(axis, stride, radix, offset))
        value = total
        done.append((axis, stride, radix, digit))
    for axis, stride, radix, digit in reversed(done):
        piece = value.shape[0]
        whole = jnp.zeros((piece * radix,) + value.shape[1:], value.dtype)
        whole = lax.dynamic_update_slice_in_dim(whole, value, digit * piece, 0)
        for offset in range(1, radix):
            got = lax.ppermute(value, axis, digit_perm(axis, stride, radix, offset))
            whole = lax.dynamic_update_slice_in_dim(whole, got, ((digit - offset) % radix) * piece, 0)
        value = whole
    return value

def body(tangents, base_flow):
    highest = lax.Precision.HIGHEST
    slope_one = tendency(add_rim(tangents, 2), base_flow)
    slope_two = tendency(add_rim(tangents + 0.5 * time_step * slope_one, 2), base_flow)
    slope_three = tendency(add_rim(tangents + 0.5 * time_step * slope_two, 2), base_flow)
    slope_four = tendency(add_rim(tangents + time_step * slope_three, 2), base_flow)
    advanced = combine_sections(tangents, slope_one, slope_two, slope_three, slope_four)
    cells = tangents.shape[0] * lax.axis_size("gx") * tangents.shape[1] * lax.axis_size("gy")
    width_vec = advanced.shape[3]
    total_vec = width_vec * lax.axis_size("vec")
    points = lax.all_to_all(advanced, "vec", split_axis=0, concat_axis=3, tiled=True)
    flat_rows = points.reshape(-1, total_vec)
    partial_value = lax.dot_general(
        flat_rows,
        flat_rows,
        (((0,), (0,)), ((), ())),
        precision=highest,
        preferred_element_type=jnp.float32,
    )
    gram_matrix = tree_sum(partial_value, reduce_groups()) / cells
    root = inverse_root(gram_matrix)
    turned = jnp.dot(
        flat_rows, root, precision=highest, preferred_element_type=jnp.float32
    ).reshape(points.shape)
    rotated = lax.all_to_all(turned, "vec", split_axis=3, concat_axis=0, tiled=True)
    return rotated


def solution(mesh):
    in_specs = (P("gx", "gy", None, "vec"), P("gx", "gy", None))
    out_specs = P("gx", "gy", None, "vec")
    return jax.shard_map(body, mesh=mesh, in_specs=in_specs, out_specs=out_specs, check_vma=False)
```

```python
import jax
import jax.numpy as jnp
from jax import lax
from jax.sharding import PartitionSpec as P

NS_ITERS = 4


time_step = 0.25
viscous = 0.05
spreading_share = 0.05
buoyancy = 1.0


def with_halo(value, sides, width, wrap):
    for axis, dim in sides:
        size, length = (lax.axis_size(axis), value.shape[dim])
        up = [(i, (i + 1) % size) for i in range(size if wrap else size - 1)]
        down = [(j, i) for i, j in up]
        last = lax.slice_in_dim(value, length - width, length, axis=dim)
        leading = lax.slice_in_dim(value, 0, width, axis=dim)
        before = lax.ppermute(last, axis, up)
        after = lax.ppermute(leading, axis, down)
        value = jnp.concatenate([before, value, after], axis=dim)
    return value


def tendency(padded, flow):
    middle_node = padded[2:-2, 2:-2]
    east_two = padded[4:, 2:-2]
    east_one = padded[3:-1, 2:-2]
    west_one = padded[1:-3, 2:-2]
    west_two = padded[:-4, 2:-2]
    north_two = padded[2:-2, 4:]
    north_one = padded[2:-2, 3:-1]
    south_one = padded[2:-2, 1:-3]
    south_two = padded[2:-2, :-4]
    deriv_x = (8.0 * (east_one - west_one) - (east_two - west_two)) / 12.0
    deriv_y = (8.0 * (north_one - south_one) - (north_two - south_two)) / 12.0
    second_derivative_sum = (
        16.0 * (east_one + west_one + north_one + south_one)
        - (east_two + west_two + north_two + south_two)
        - 60.0 * middle_node
    ) / 12.0
    vel_x = flow[:, :, 0][:, :, None, None]
    vel_y = flow[:, :, 1][:, :, None, None]
    thermal_forcing = flow[:, :, 2][:, :, None]
    transport_share = -(vel_x * deriv_x + vel_y * deriv_y)
    swirl_profile = (
        transport_share[:, :, 0]
        + viscous * second_derivative_sum[:, :, 0]
        + buoyancy * deriv_x[:, :, 1]
    )
    heat_profile = (
        transport_share[:, :, 1]
        + spreading_share * second_derivative_sum[:, :, 1]
        + thermal_forcing * middle_node[:, :, 0]
    )
    return jnp.stack([swirl_profile, heat_profile], axis=2)


def combine_sections(field, slope_one, slope_two, slope_three, slope_four):
    return field + time_step / 6.0 * (slope_one + 2.0 * slope_two + 2.0 * slope_three + slope_four)


def add_rim(field, width):
    wider = with_halo(field, (("gx", 0),), width, True)
    side = with_halo(field, (("gy", 1),), width, False)
    below = jnp.pad(side[:, :width], ((width, width),) + ((0, 0),) * (field.ndim - 1))
    above = jnp.pad(side[:, -width:], ((width, width),) + ((0, 0),) * (field.ndim - 1))
    return jnp.concatenate([below, wider, above], axis=1)


def inverse_root(gram_matrix):
    highest = lax.Precision.HIGHEST
    scale_norm = jnp.sqrt(jnp.sum(gram_matrix * gram_matrix) + 1e-06)
    identity = jnp.eye(gram_matrix.shape[0], dtype=jnp.float32)
    iterate_y = gram_matrix / scale_norm
    iterate_z = None
    for iteration in range(NS_ITERS):
        if iterate_z is None:
            product = iterate_y
        else:
            product = jnp.dot(iterate_z, iterate_y, precision=highest, preferred_element_type=jnp.float32)
        poly = 1.5 * identity - 0.5 * product
        if iteration + 1 < NS_ITERS:
            iterate_y = jnp.dot(iterate_y, poly, precision=highest, preferred_element_type=jnp.float32)
        if iterate_z is None:
            iterate_z = poly
        else:
            iterate_z = jnp.dot(poly, iterate_z, precision=highest, preferred_element_type=jnp.float32)
    return iterate_z / jnp.sqrt(scale_norm)


def reduce_groups():
    groups = []
    for axis in ("gy", "vec", "gx"):
        size = lax.axis_size(axis)
        assert size & (size - 1) == 0
        stride = 1
        if axis == "gy" and size > 1:
            groups.append((axis, 1, 2))
            stride = 2
        while stride < size:
            radix = 2 if axis == "gx" and stride == 1 and size > 4 else min(4, size // stride)
            groups.append((axis, stride, radix))
            stride *= radix
    scatter = [group for group in groups if group[0] != "gx"]
    whole = [group for group in groups if group[0] == "gx"]
    return scatter, whole


def digit_perm(axis, stride, radix, offset):
    pairs = []
    for i in range(lax.axis_size(axis)):
        digit = (i // stride) % radix
        pairs.append((i, i + (((digit + offset) % radix) - digit) * stride))
    return pairs


def tree_sum(value, groups):
    scatter, whole_groups = groups
    done = []
    for axis, stride, radix in scatter:
        piece = value.shape[0] // radix
        digit = (lax.axis_index(axis) // stride) % radix
        total = lax.dynamic_slice_in_dim(value, digit * piece, piece, 0)
        for offset in range(1, radix):
            send = lax.dynamic_slice_in_dim(value, ((digit + offset) % radix) * piece, piece, 0)
            total = total + lax.ppermute(send, axis, digit_perm(axis, stride, radix, offset))
        value = total
        done.append((axis, stride, radix, digit))
    for axis, stride, radix in whole_groups:
        digit = (lax.axis_index(axis) // stride) % radix
        arrived = [value] + [
            lax.ppermute(value, axis, digit_perm(axis, stride, radix, offset)) for offset in range(1, radix)
        ]
        stacked = jnp.stack(arrived)
        value = lax.dynamic_index_in_dim(stacked, digit % radix, keepdims=False)
        for source in range(1, radix):
            value = value + lax.dynamic_index_in_dim(stacked, (digit - source) % radix, keepdims=False)
    for axis, stride, radix, digit in reversed(done):
        piece = value.shape[0]
        whole = jnp.zeros((piece * radix,) + value.shape[1:], value.dtype)
        whole = lax.dynamic_update_slice_in_dim(whole, value, digit * piece, 0)
        for offset in range(1, radix):
            got = lax.ppermute(value, axis, digit_perm(axis, stride, radix, offset))
            whole = lax.dynamic_update_slice_in_dim(whole, got, ((digit - offset) % radix) * piece, 0)
        value = whole
    return value

def body(tangents, base_flow):
    highest = lax.Precision.HIGHEST
    slope_one = tendency(add_rim(tangents, 2), base_flow)
    slope_two = tendency(add_rim(tangents + 0.5 * time_step * slope_one, 2), base_flow)
    slope_three = tendency(add_rim(tangents + 0.5 * time_step * slope_two, 2), base_flow)
    slope_four = tendency(add_rim(tangents + time_step * slope_three, 2), base_flow)
    advanced = combine_sections(tangents, slope_one, slope_two, slope_three, slope_four)
    cells = tangents.shape[0] * lax.axis_size("gx") * tangents.shape[1] * lax.axis_size("gy")
    width_vec = advanced.shape[3]
    total_vec = width_vec * lax.axis_size("vec")
    points = lax.all_to_all(advanced, "vec", split_axis=0, concat_axis=3, tiled=True)
    flat_rows = points.reshape(-1, total_vec)
    partial_value = lax.dot_general(
        flat_rows,
        flat_rows,
        (((0,), (0,)), ((), ())),
        precision=highest,
        preferred_element_type=jnp.float32,
    )
    gram_matrix = tree_sum(partial_value, reduce_groups()) / cells
    root = inverse_root(gram_matrix)
    parts = lax.axis_size("vec")
    me = lax.axis_index("vec")
    rows = points.shape[0]
    rotated = jnp.zeros(tangents.shape, tangents.dtype)
    for offset in range(parts):
        target = (me + offset) % parts
        columns = lax.dynamic_slice_in_dim(root, target * width_vec, width_vec, 1)
        turned = jnp.dot(flat_rows, columns, precision=highest, preferred_element_type=jnp.float32)
        turned = turned.reshape(points.shape[:3] + (width_vec,))
        if offset:
            turned = lax.ppermute(turned, "vec", digit_perm("vec", 1, parts, offset))
        source = (me - offset) % parts
        rotated = lax.dynamic_update_slice_in_dim(rotated, turned, source * rows, 0)
    return rotated


def solution(mesh):
    in_specs = (P("gx", "gy", None, "vec"), P("gx", "gy", None))
    out_specs = P("gx", "gy", None, "vec")
    return jax.shard_map(body, mesh=mesh, in_specs=in_specs, out_specs=out_specs, check_vma=False)
```

```python
import jax
import jax.numpy as jnp
from jax import lax
from jax.sharding import PartitionSpec as P

NS_ITERS = 4


time_step = 0.25
viscous = 0.05
spreading_share = 0.05
buoyancy = 1.0


def with_halo(value, sides, width, wrap):
    for axis, dim in sides:
        size, length = (lax.axis_size(axis), value.shape[dim])
        up = [(i, (i + 1) % size) for i in range(size if wrap else size - 1)]
        down = [(j, i) for i, j in up]
        last = lax.slice_in_dim(value, length - width, length, axis=dim)
        leading = lax.slice_in_dim(value, 0, width, axis=dim)
        before = lax.ppermute(last, axis, up)
        after = lax.ppermute(leading, axis, down)
        value = jnp.concatenate([before, value, after], axis=dim)
    return value


def tendency(padded, flow):
    middle_node = padded[2:-2, 2:-2]
    east_two = padded[4:, 2:-2]
    east_one = padded[3:-1, 2:-2]
    west_one = padded[1:-3, 2:-2]
    west_two = padded[:-4, 2:-2]
    north_two = padded[2:-2, 4:]
    north_one = padded[2:-2, 3:-1]
    south_one = padded[2:-2, 1:-3]
    south_two = padded[2:-2, :-4]
    deriv_x = (8.0 * (east_one - west_one) - (east_two - west_two)) / 12.0
    deriv_y = (8.0 * (north_one - south_one) - (north_two - south_two)) / 12.0
    second_derivative_sum = (
        16.0 * (east_one + west_one + north_one + south_one)
        - (east_two + west_two + north_two + south_two)
        - 60.0 * middle_node
    ) / 12.0
    vel_x = flow[:, :, 0][:, :, None, None]
    vel_y = flow[:, :, 1][:, :, None, None]
    thermal_forcing = flow[:, :, 2][:, :, None]
    transport_share = -(vel_x * deriv_x + vel_y * deriv_y)
    swirl_profile = (
        transport_share[:, :, 0]
        + viscous * second_derivative_sum[:, :, 0]
        + buoyancy * deriv_x[:, :, 1]
    )
    heat_profile = (
        transport_share[:, :, 1]
        + spreading_share * second_derivative_sum[:, :, 1]
        + thermal_forcing * middle_node[:, :, 0]
    )
    return jnp.stack([swirl_profile, heat_profile], axis=2)


def combine_sections(field, slope_one, slope_two, slope_three, slope_four):
    return field + time_step / 6.0 * (slope_one + 2.0 * slope_two + 2.0 * slope_three + slope_four)


def add_rim(field, width):
    wider = with_halo(field, (("gx", 0),), width, True)
    side = with_halo(field, (("gy", 1),), width, False)
    below = jnp.pad(side[:, :width], ((width, width),) + ((0, 0),) * (field.ndim - 1))
    above = jnp.pad(side[:, -width:], ((width, width),) + ((0, 0),) * (field.ndim - 1))
    return jnp.concatenate([below, wider, above], axis=1)


def inverse_root(gram_matrix):
    highest = lax.Precision.HIGH
    scale_norm = jnp.sqrt(jnp.sum(gram_matrix * gram_matrix) + 1e-06)
    identity = jnp.eye(gram_matrix.shape[0], dtype=jnp.float32)
    iterate_y = gram_matrix / scale_norm
    iterate_z = None
    for iteration in range(NS_ITERS):
        if iterate_z is None:
            product = iterate_y
        else:
            product = jnp.dot(iterate_z, iterate_y, precision=highest, preferred_element_type=jnp.float32)
        poly = 1.5 * identity - 0.5 * product
        if iteration + 1 < NS_ITERS:
            iterate_y = jnp.dot(iterate_y, poly, precision=highest, preferred_element_type=jnp.float32)
        if iterate_z is None:
            iterate_z = poly
        else:
            iterate_z = jnp.dot(poly, iterate_z, precision=highest, preferred_element_type=jnp.float32)
    return iterate_z / jnp.sqrt(scale_norm)


def reduce_groups():
    groups = []
    for axis in ("gy", "vec", "gx"):
        size = lax.axis_size(axis)
        assert size & (size - 1) == 0
        stride = 1
        if axis == "gy" and size > 1:
            groups.append((axis, 1, 2))
            stride = 2
        while stride < size:
            radix = 2 if axis == "gx" and stride == 1 and size > 4 else min(4, size // stride)
            groups.append((axis, stride, radix))
            stride *= radix
    scatter = [group for group in groups if group[0] != "gx"]
    whole = [group for group in groups if group[0] == "gx"]
    return scatter, whole


def digit_perm(axis, stride, radix, offset):
    pairs = []
    for i in range(lax.axis_size(axis)):
        digit = (i // stride) % radix
        pairs.append((i, i + (((digit + offset) % radix) - digit) * stride))
    return pairs


def tree_sum(value, groups):
    scatter, whole_groups = groups
    done = []
    for axis, stride, radix in scatter:
        piece = value.shape[0] // radix
        digit = (lax.axis_index(axis) // stride) % radix
        total = lax.dynamic_slice_in_dim(value, digit * piece, piece, 0)
        for offset in range(1, radix):
            send = lax.dynamic_slice_in_dim(value, ((digit + offset) % radix) * piece, piece, 0)
            total = total + lax.ppermute(send, axis, digit_perm(axis, stride, radix, offset))
        value = total
        done.append((axis, stride, radix, digit))
    for axis, stride, radix in whole_groups:
        digit = (lax.axis_index(axis) // stride) % radix
        arrived = [value] + [
            lax.ppermute(value, axis, digit_perm(axis, stride, radix, offset)) for offset in range(1, radix)
        ]
        stacked = jnp.stack(arrived)
        value = lax.dynamic_index_in_dim(stacked, digit % radix, keepdims=False)
        for source in range(1, radix):
            value = value + lax.dynamic_index_in_dim(stacked, (digit - source) % radix, keepdims=False)
    for axis, stride, radix, digit in reversed(done):
        piece = value.shape[0]
        whole = jnp.zeros((piece * radix,) + value.shape[1:], value.dtype)
        whole = lax.dynamic_update_slice_in_dim(whole, value, digit * piece, 0)
        for offset in range(1, radix):
            got = lax.ppermute(value, axis, digit_perm(axis, stride, radix, offset))
            whole = lax.dynamic_update_slice_in_dim(whole, got, ((digit - offset) % radix) * piece, 0)
        value = whole
    return value

def body(tangents, base_flow):
    highest = lax.Precision.HIGHEST
    slope_one = tendency(add_rim(tangents, 2), base_flow)
    slope_two = tendency(add_rim(tangents + 0.5 * time_step * slope_one, 2), base_flow)
    slope_three = tendency(add_rim(tangents + 0.5 * time_step * slope_two, 2), base_flow)
    slope_four = tendency(add_rim(tangents + time_step * slope_three, 2), base_flow)
    advanced = combine_sections(tangents, slope_one, slope_two, slope_three, slope_four)
    cells = tangents.shape[0] * lax.axis_size("gx") * tangents.shape[1] * lax.axis_size("gy")
    width_vec = advanced.shape[3]
    total_vec = width_vec * lax.axis_size("vec")
    points = lax.all_to_all(advanced, "vec", split_axis=0, concat_axis=3, tiled=True)
    flat_rows = points.reshape(-1, total_vec)
    partial_value = lax.dot_general(
        flat_rows,
        flat_rows,
        (((0,), (0,)), ((), ())),
        precision=highest,
        preferred_element_type=jnp.float32,
    )
    gram_matrix = tree_sum(partial_value, reduce_groups()) / cells
    root = inverse_root(gram_matrix)
    parts = lax.axis_size("vec")
    me = lax.axis_index("vec")
    rows = points.shape[0]
    rotated = jnp.zeros(tangents.shape, tangents.dtype)
    for offset in range(parts):
        target = (me + offset) % parts
        columns = lax.dynamic_slice_in_dim(root, target * width_vec, width_vec, 1)
        turned = jnp.dot(flat_rows, columns, precision=highest, preferred_element_type=jnp.float32)
        turned = turned.reshape(points.shape[:3] + (width_vec,))
        if offset:
            turned = lax.ppermute(turned, "vec", digit_perm("vec", 1, parts, offset))
        source = (me - offset) % parts
        rotated = lax.dynamic_update_slice_in_dim(rotated, turned, source * rows, 0)
    return rotated


def solution(mesh):
    in_specs = (P("gx", "gy", None, "vec"), P("gx", "gy", None))
    out_specs = P("gx", "gy", None, "vec")
    return jax.shard_map(body, mesh=mesh, in_specs=in_specs, out_specs=out_specs, check_vma=False)
```

```python
import jax
import jax.numpy as jnp
from jax import lax
from jax.sharding import PartitionSpec as P

NS_ITERS = 4


time_step = 0.25
viscous = 0.05
spreading_share = 0.05
buoyancy = 1.0


def with_halo(value, sides, width, wrap):
    for axis, dim in sides:
        size, length = (lax.axis_size(axis), value.shape[dim])
        up = [(i, (i + 1) % size) for i in range(size if wrap else size - 1)]
        down = [(j, i) for i, j in up]
        last = lax.slice_in_dim(value, length - width, length, axis=dim)
        leading = lax.slice_in_dim(value, 0, width, axis=dim)
        before = lax.ppermute(last, axis, up)
        after = lax.ppermute(leading, axis, down)
        value = jnp.concatenate([before, value, after], axis=dim)
    return value


def tendency(padded, flow):
    middle_node = padded[2:-2, 2:-2]
    east_two = padded[4:, 2:-2]
    east_one = padded[3:-1, 2:-2]
    west_one = padded[1:-3, 2:-2]
    west_two = padded[:-4, 2:-2]
    north_two = padded[2:-2, 4:]
    north_one = padded[2:-2, 3:-1]
    south_one = padded[2:-2, 1:-3]
    south_two = padded[2:-2, :-4]
    deriv_x = (8.0 * (east_one - west_one) - (east_two - west_two)) / 12.0
    deriv_y = (8.0 * (north_one - south_one) - (north_two - south_two)) / 12.0
    second_derivative_sum = (
        16.0 * (east_one + west_one + north_one + south_one)
        - (east_two + west_two + north_two + south_two)
        - 60.0 * middle_node
    ) / 12.0
    vel_x = flow[:, :, 0][:, :, None, None]
    vel_y = flow[:, :, 1][:, :, None, None]
    thermal_forcing = flow[:, :, 2][:, :, None]
    transport_share = -(vel_x * deriv_x + vel_y * deriv_y)
    swirl_profile = (
        transport_share[:, :, 0]
        + viscous * second_derivative_sum[:, :, 0]
        + buoyancy * deriv_x[:, :, 1]
    )
    heat_profile = (
        transport_share[:, :, 1]
        + spreading_share * second_derivative_sum[:, :, 1]
        + thermal_forcing * middle_node[:, :, 0]
    )
    return jnp.stack([swirl_profile, heat_profile], axis=2)


def combine_sections(field, slope_one, slope_two, slope_three, slope_four):
    return field + time_step / 6.0 * (slope_one + 2.0 * slope_two + 2.0 * slope_three + slope_four)


def add_rim(field, width):
    wider = with_halo(field, (("gx", 0),), width, True)
    side = with_halo(field, (("gy", 1),), width, False)
    below = jnp.pad(side[:, :width], ((width, width),) + ((0, 0),) * (field.ndim - 1))
    above = jnp.pad(side[:, -width:], ((width, width),) + ((0, 0),) * (field.ndim - 1))
    return jnp.concatenate([below, wider, above], axis=1)


def moved(piece, dx, dy):
    nx, ny = lax.axis_size("gx"), lax.axis_size("gy")
    if dy == 0:
        return lax.ppermute(piece, "gx", [(a, (a + dx) % nx) for a in range(nx)])
    if dx == 0:
        return lax.ppermute(piece, "gy", [(b, b + dy) for b in range(ny) if 0 <= b + dy < ny])
    pairs = [(a * ny + b, ((a + dx) % nx) * ny + b + dy) for a in range(nx) for b in range(ny) if 0 <= b + dy < ny]
    return lax.ppermute(piece, ("gx", "gy"), pairs)


def with_frame(field, width):
    w = width
    before_x = moved(field[-w:], 1, 0)
    after_x = moved(field[:w], -1, 0)
    before_y = moved(field[:, -w:], 0, 1)
    after_y = moved(field[:, :w], 0, -1)
    corner_bb = moved(field[-w:, -w:], 1, 1)
    corner_ba = moved(field[-w:, :w], 1, -1)
    corner_ab = moved(field[:w, -w:], -1, 1)
    corner_aa = moved(field[:w, :w], -1, -1)
    top = jnp.concatenate([corner_bb, before_x, corner_ba], axis=1)
    middle = jnp.concatenate([before_y, field, after_y], axis=1)
    bottom = jnp.concatenate([corner_ab, after_x, corner_aa], axis=1)
    return jnp.concatenate([top, middle, bottom], axis=0)


def inside_walls(columns, margin):
    first = lax.axis_index("gy") * (columns - 2 * margin) - margin
    place = first + lax.broadcasted_iota(jnp.int32, (1, columns, 1, 1), 1)
    total = (columns - 2 * margin) * lax.axis_size("gy")
    return ((place >= 0) & (place < total)).astype(jnp.float32)


def inverse_root(gram_matrix):
    highest = lax.Precision.HIGH
    scale_norm = jnp.sqrt(jnp.sum(gram_matrix * gram_matrix) + 1e-06)
    identity = jnp.eye(gram_matrix.shape[0], dtype=jnp.float32)
    iterate_y = gram_matrix / scale_norm
    iterate_z = None
    for iteration in range(NS_ITERS):
        if iterate_z is None:
            product = iterate_y
        else:
            product = jnp.dot(iterate_z, iterate_y, precision=highest, preferred_element_type=jnp.float32)
        poly = 1.5 * identity - 0.5 * product
        if iteration + 1 < NS_ITERS:
            iterate_y = jnp.dot(iterate_y, poly, precision=highest, preferred_element_type=jnp.float32)
        if iterate_z is None:
            iterate_z = poly
        else:
            iterate_z = jnp.dot(poly, iterate_z, precision=highest, preferred_element_type=jnp.float32)
    return iterate_z / jnp.sqrt(scale_norm)


def reduce_groups():
    groups = []
    for axis in ("gy", "vec", "gx"):
        size = lax.axis_size(axis)
        assert size & (size - 1) == 0
        stride = 1
        if axis == "gy" and size > 1:
            groups.append((axis, 1, 2))
            stride = 2
        while stride < size:
            radix = 2 if axis == "gx" and stride == 1 and size > 4 else min(4, size // stride)
            groups.append((axis, stride, radix))
            stride *= radix
    scatter = [group for group in groups if group[0] != "gx"]
    whole = [group for group in groups if group[0] == "gx"]
    return scatter, whole


def digit_perm(axis, stride, radix, offset):
    pairs = []
    for i in range(lax.axis_size(axis)):
        digit = (i // stride) % radix
        pairs.append((i, i + (((digit + offset) % radix) - digit) * stride))
    return pairs


def tree_sum(value, groups):
    scatter, whole_groups = groups
    done = []
    for axis, stride, radix in scatter:
        piece = value.shape[0] // radix
        digit = (lax.axis_index(axis) // stride) % radix
        total = lax.dynamic_slice_in_dim(value, digit * piece, piece, 0)
        for offset in range(1, radix):
            send = lax.dynamic_slice_in_dim(value, ((digit + offset) % radix) * piece, piece, 0)
            total = total + lax.ppermute(send, axis, digit_perm(axis, stride, radix, offset))
        value = total
        done.append((axis, stride, radix, digit))
    for axis, stride, radix in whole_groups:
        digit = (lax.axis_index(axis) // stride) % radix
        arrived = [value] + [
            lax.ppermute(value, axis, digit_perm(axis, stride, radix, offset)) for offset in range(1, radix)
        ]
        stacked = jnp.stack(arrived)
        value = lax.dynamic_index_in_dim(stacked, digit % radix, keepdims=False)
        for source in range(1, radix):
            value = value + lax.dynamic_index_in_dim(stacked, (digit - source) % radix, keepdims=False)
    for axis, stride, radix, digit in reversed(done):
        piece = value.shape[0]
        whole = jnp.zeros((piece * radix,) + value.shape[1:], value.dtype)
        whole = lax.dynamic_update_slice_in_dim(whole, value, digit * piece, 0)
        for offset in range(1, radix):
            got = lax.ppermute(value, axis, digit_perm(axis, stride, radix, offset))
            whole = lax.dynamic_update_slice_in_dim(whole, got, ((digit - offset) % radix) * piece, 0)
        value = whole
    return value

def body(tangents, base_flow):
    highest = lax.Precision.HIGHEST
    flow_framed = with_frame(base_flow, 2)
    walls = inside_walls(tangents.shape[1] + 4, 2)
    field_framed = with_frame(tangents, 4)
    slope_one_framed = tendency(field_framed, flow_framed)
    slope_one = slope_one_framed[2:-2, 2:-2]
    field_ring = field_framed[2:-2, 2:-2]
    slope_two = tendency((field_ring + 0.5 * time_step * slope_one_framed) * walls, base_flow)
    second_framed = with_frame(tangents + 0.5 * time_step * slope_two, 4)
    slope_three_framed = tendency(second_framed, flow_framed)
    slope_three = slope_three_framed[2:-2, 2:-2]
    slope_four = tendency((field_ring + time_step * slope_three_framed) * walls, base_flow)
    advanced = combine_sections(tangents, slope_one, slope_two, slope_three, slope_four)
    cells = tangents.shape[0] * lax.axis_size("gx") * tangents.shape[1] * lax.axis_size("gy")
    width_vec = advanced.shape[3]
    total_vec = width_vec * lax.axis_size("vec")
    points = lax.all_to_all(advanced, "vec", split_axis=0, concat_axis=3, tiled=True)
    flat_rows = points.reshape(-1, total_vec)
    partial_value = lax.dot_general(
        flat_rows,
        flat_rows,
        (((0,), (0,)), ((), ())),
        precision=highest,
        preferred_element_type=jnp.float32,
    )
    gram_matrix = tree_sum(partial_value, reduce_groups()) / cells
    root = inverse_root(gram_matrix)
    parts = lax.axis_size("vec")
    me = lax.axis_index("vec")
    rows = points.shape[0]
    rotated = jnp.zeros(tangents.shape, tangents.dtype)
    for offset in range(parts):
        target = (me + offset) % parts
        columns = lax.dynamic_slice_in_dim(root, target * width_vec, width_vec, 1)
        turned = jnp.dot(flat_rows, columns, precision=highest, preferred_element_type=jnp.float32)
        turned = turned.reshape(points.shape[:3] + (width_vec,))
        if offset:
            turned = lax.ppermute(turned, "vec", digit_perm("vec", 1, parts, offset))
        source = (me - offset) % parts
        rotated = lax.dynamic_update_slice_in_dim(rotated, turned, source * rows, 0)
    return rotated


def solution(mesh):
    in_specs = (P("gx", "gy", None, "vec"), P("gx", "gy", None))
    out_specs = P("gx", "gy", None, "vec")
    return jax.shard_map(body, mesh=mesh, in_specs=in_specs, out_specs=out_specs, check_vma=False)
```

```python
import jax
import jax.numpy as jnp
from jax import lax
from jax.sharding import PartitionSpec as P

NS_ITERS = 4


time_step = 0.25
viscous = 0.05
spreading_share = 0.05
buoyancy = 1.0


def with_halo(value, sides, width, wrap):
    for axis, dim in sides:
        size, length = (lax.axis_size(axis), value.shape[dim])
        up = [(i, (i + 1) % size) for i in range(size if wrap else size - 1)]
        down = [(j, i) for i, j in up]
        last = lax.slice_in_dim(value, length - width, length, axis=dim)
        leading = lax.slice_in_dim(value, 0, width, axis=dim)
        before = lax.ppermute(last, axis, up)
        after = lax.ppermute(leading, axis, down)
        value = jnp.concatenate([before, value, after], axis=dim)
    return value


def tendency(padded, flow):
    middle_node = padded[2:-2, 2:-2]
    east_two = padded[4:, 2:-2]
    east_one = padded[3:-1, 2:-2]
    west_one = padded[1:-3, 2:-2]
    west_two = padded[:-4, 2:-2]
    north_two = padded[2:-2, 4:]
    north_one = padded[2:-2, 3:-1]
    south_one = padded[2:-2, 1:-3]
    south_two = padded[2:-2, :-4]
    deriv_x = (8.0 * (east_one - west_one) - (east_two - west_two)) / 12.0
    deriv_y = (8.0 * (north_one - south_one) - (north_two - south_two)) / 12.0
    second_derivative_sum = (
        16.0 * (east_one + west_one + north_one + south_one)
        - (east_two + west_two + north_two + south_two)
        - 60.0 * middle_node
    ) / 12.0
    vel_x = flow[:, :, 0][:, :, None, None]
    vel_y = flow[:, :, 1][:, :, None, None]
    thermal_forcing = flow[:, :, 2][:, :, None]
    transport_share = -(vel_x * deriv_x + vel_y * deriv_y)
    swirl_profile = (
        transport_share[:, :, 0]
        + viscous * second_derivative_sum[:, :, 0]
        + buoyancy * deriv_x[:, :, 1]
    )
    heat_profile = (
        transport_share[:, :, 1]
        + spreading_share * second_derivative_sum[:, :, 1]
        + thermal_forcing * middle_node[:, :, 0]
    )
    return jnp.stack([swirl_profile, heat_profile], axis=2)


def combine_sections(field, slope_one, slope_two, slope_three, slope_four):
    return field + time_step / 6.0 * (slope_one + 2.0 * slope_two + 2.0 * slope_three + slope_four)


def add_rim(field, width):
    wider = with_halo(field, (("gx", 0),), width, True)
    side = with_halo(field, (("gy", 1),), width, False)
    below = jnp.pad(side[:, :width], ((width, width),) + ((0, 0),) * (field.ndim - 1))
    above = jnp.pad(side[:, -width:], ((width, width),) + ((0, 0),) * (field.ndim - 1))
    return jnp.concatenate([below, wider, above], axis=1)


def inverse_root(gram_matrix):
    highest = lax.Precision.HIGH
    scale_norm = jnp.sqrt(jnp.sum(gram_matrix * gram_matrix) + 1e-06)
    identity = jnp.eye(gram_matrix.shape[0], dtype=jnp.float32)
    iterate_y = gram_matrix / scale_norm
    iterate_z = None
    for iteration in range(NS_ITERS):
        if iterate_z is None:
            product = iterate_y
        else:
            product = jnp.dot(iterate_z, iterate_y, precision=highest, preferred_element_type=jnp.float32)
        poly = 1.5 * identity - 0.5 * product
        if iterate_z is None:
            iterate_y = jnp.dot(iterate_y, poly, precision=highest, preferred_element_type=jnp.float32)
            iterate_z = poly
        elif iteration + 1 < NS_ITERS:
            both = jnp.dot(
                jnp.concatenate([iterate_y, iterate_z], 0), poly, precision=highest, preferred_element_type=jnp.float32
            )
            iterate_y, iterate_z = both[: poly.shape[0]], both[poly.shape[0] :]
        else:
            iterate_z = jnp.dot(iterate_z, poly, precision=highest, preferred_element_type=jnp.float32)
    return iterate_z / jnp.sqrt(scale_norm)


def reduce_groups():
    groups = []
    for axis in ("gy", "vec", "gx"):
        size = lax.axis_size(axis)
        assert size & (size - 1) == 0
        stride = 1
        if axis == "gy" and size > 1:
            groups.append((axis, 1, 2))
            stride = 2
        while stride < size:
            radix = 2 if axis == "gx" and stride == 1 and size > 4 else min(4, size // stride)
            groups.append((axis, stride, radix))
            stride *= radix
    scatter = [group for group in groups if group[0] != "gx"]
    whole = [group for group in groups if group[0] == "gx"]
    return scatter, whole


def digit_perm(axis, stride, radix, offset):
    pairs = []
    for i in range(lax.axis_size(axis)):
        digit = (i // stride) % radix
        pairs.append((i, i + (((digit + offset) % radix) - digit) * stride))
    return pairs


def tree_sum(value, groups):
    scatter, whole_groups = groups
    done = []
    for axis, stride, radix in scatter:
        piece = value.shape[0] // radix
        digit = (lax.axis_index(axis) // stride) % radix
        total = lax.dynamic_slice_in_dim(value, digit * piece, piece, 0)
        for offset in range(1, radix):
            send = lax.dynamic_slice_in_dim(value, ((digit + offset) % radix) * piece, piece, 0)
            total = total + lax.ppermute(send, axis, digit_perm(axis, stride, radix, offset))
        value = total
        done.append((axis, stride, radix, digit))
    for axis, stride, radix in whole_groups:
        digit = (lax.axis_index(axis) // stride) % radix
        arrived = [value] + [
            lax.ppermute(value, axis, digit_perm(axis, stride, radix, offset)) for offset in range(1, radix)
        ]
        stacked = jnp.stack(arrived)
        value = lax.dynamic_index_in_dim(stacked, digit % radix, keepdims=False)
        for source in range(1, radix):
            value = value + lax.dynamic_index_in_dim(stacked, (digit - source) % radix, keepdims=False)
    for axis, stride, radix, digit in reversed(done):
        piece = value.shape[0]
        whole = jnp.zeros((piece * radix,) + value.shape[1:], value.dtype)
        whole = lax.dynamic_update_slice_in_dim(whole, value, digit * piece, 0)
        for offset in range(1, radix):
            got = lax.ppermute(value, axis, digit_perm(axis, stride, radix, offset))
            whole = lax.dynamic_update_slice_in_dim(whole, got, ((digit - offset) % radix) * piece, 0)
        value = whole
    return value

def body(tangents, base_flow):
    highest = lax.Precision.HIGH
    slope_one = tendency(add_rim(tangents, 2), base_flow)
    slope_two = tendency(add_rim(tangents + 0.5 * time_step * slope_one, 2), base_flow)
    slope_three = tendency(add_rim(tangents + 0.5 * time_step * slope_two, 2), base_flow)
    slope_four = tendency(add_rim(tangents + time_step * slope_three, 2), base_flow)
    advanced = combine_sections(tangents, slope_one, slope_two, slope_three, slope_four)
    cells = tangents.shape[0] * lax.axis_size("gx") * tangents.shape[1] * lax.axis_size("gy")
    width_vec = advanced.shape[3]
    total_vec = width_vec * lax.axis_size("vec")
    points = lax.all_to_all(advanced, "vec", split_axis=0, concat_axis=3, tiled=True)
    flat_rows = points.reshape(-1, total_vec)
    partial_value = lax.dot_general(
        flat_rows,
        flat_rows,
        (((0,), (0,)), ((), ())),
        precision=highest,
        preferred_element_type=jnp.float32,
    )
    gram_matrix = tree_sum(partial_value, reduce_groups()) / cells
    root = inverse_root(gram_matrix)
    parts = lax.axis_size("vec")
    me = lax.axis_index("vec")
    rows = points.shape[0]
    rotated = jnp.zeros(tangents.shape, tangents.dtype)
    for offset in range(parts):
        target = (me + offset) % parts
        columns = lax.dynamic_slice_in_dim(root, target * width_vec, width_vec, 1)
        turned = jnp.dot(flat_rows, columns, precision=highest, preferred_element_type=jnp.float32)
        turned = turned.reshape(points.shape[:3] + (width_vec,))
        if offset:
            turned = lax.ppermute(turned, "vec", digit_perm("vec", 1, parts, offset))
        source = (me - offset) % parts
        rotated = lax.dynamic_update_slice_in_dim(rotated, turned, source * rows, 0)
    return rotated


def solution(mesh):
    in_specs = (P("gx", "gy", None, "vec"), P("gx", "gy", None))
    out_specs = P("gx", "gy", None, "vec")
    return jax.shard_map(body, mesh=mesh, in_specs=in_specs, out_specs=out_specs, check_vma=False)
```

```python
import jax
import jax.numpy as jnp
from jax import lax
from jax.sharding import PartitionSpec as P

NS_ITERS = 4


time_step = 0.25
viscous = 0.05
spreading_share = 0.05
buoyancy = 1.0


def with_halo(value, sides, width, wrap):
    for axis, dim in sides:
        size, length = (lax.axis_size(axis), value.shape[dim])
        up = [(i, (i + 1) % size) for i in range(size if wrap else size - 1)]
        down = [(j, i) for i, j in up]
        last = lax.slice_in_dim(value, length - width, length, axis=dim)
        leading = lax.slice_in_dim(value, 0, width, axis=dim)
        before = lax.ppermute(last, axis, up)
        after = lax.ppermute(leading, axis, down)
        value = jnp.concatenate([before, value, after], axis=dim)
    return value


def tendency(padded, flow):
    middle_node = padded[2:-2, 2:-2]
    east_two = padded[4:, 2:-2]
    east_one = padded[3:-1, 2:-2]
    west_one = padded[1:-3, 2:-2]
    west_two = padded[:-4, 2:-2]
    north_two = padded[2:-2, 4:]
    north_one = padded[2:-2, 3:-1]
    south_one = padded[2:-2, 1:-3]
    south_two = padded[2:-2, :-4]
    deriv_x = (8.0 * (east_one - west_one) - (east_two - west_two)) / 12.0
    deriv_y = (8.0 * (north_one - south_one) - (north_two - south_two)) / 12.0
    second_derivative_sum = (
        16.0 * (east_one + west_one + north_one + south_one)
        - (east_two + west_two + north_two + south_two)
        - 60.0 * middle_node
    ) / 12.0
    vel_x = flow[:, :, 0][:, :, None, None]
    vel_y = flow[:, :, 1][:, :, None, None]
    thermal_forcing = flow[:, :, 2][:, :, None, None]
    transport_share = -(vel_x * deriv_x + vel_y * deriv_y)
    spread = jnp.array([viscous, spreading_share], jnp.float32)[:, None]
    coupling = jnp.concatenate(
        [buoyancy * deriv_x[:, :, 1:2], thermal_forcing * middle_node[:, :, 0:1]], axis=2
    )
    return transport_share + spread * second_derivative_sum + coupling


def combine_sections(field, slope_one, slope_two, slope_three, slope_four):
    return field + time_step / 6.0 * (slope_one + 2.0 * slope_two + 2.0 * slope_three + slope_four)


def add_rim(field, width):
    wider = with_halo(field, (("gx", 0),), width, True)
    side = with_halo(field, (("gy", 1),), width, False)
    below = jnp.pad(side[:, :width], ((width, width),) + ((0, 0),) * (field.ndim - 1))
    above = jnp.pad(side[:, -width:], ((width, width),) + ((0, 0),) * (field.ndim - 1))
    return jnp.concatenate([below, wider, above], axis=1)


def inverse_root(gram_matrix):
    highest = lax.Precision.HIGH
    scale_norm = jnp.sqrt(jnp.sum(gram_matrix * gram_matrix) + 1e-06)
    identity = jnp.eye(gram_matrix.shape[0], dtype=jnp.float32)
    iterate_y = gram_matrix / scale_norm
    iterate_z = None
    for iteration in range(NS_ITERS):
        if iterate_z is None:
            product = iterate_y
        else:
            product = jnp.dot(iterate_z, iterate_y, precision=highest, preferred_element_type=jnp.float32)
        poly = 1.5 * identity - 0.5 * product
        if iteration + 1 < NS_ITERS:
            iterate_y = jnp.dot(iterate_y, poly, precision=highest, preferred_element_type=jnp.float32)
        if iterate_z is None:
            iterate_z = poly
        else:
            iterate_z = jnp.dot(poly, iterate_z, precision=highest, preferred_element_type=jnp.float32)
    return iterate_z / jnp.sqrt(scale_norm)


def reduce_groups():
    groups = []
    for axis in ("gy", "vec", "gx"):
        size = lax.axis_size(axis)
        assert size & (size - 1) == 0
        stride = 1
        if axis == "gy" and size > 1:
            groups.append((axis, 1, 2))
            stride = 2
        while stride < size:
            radix = 2 if axis == "gx" and stride == 1 and size > 4 else min(4, size // stride)
            groups.append((axis, stride, radix))
            stride *= radix
    scatter = [group for group in groups if group[0] != "gx"]
    whole = [group for group in groups if group[0] == "gx"]
    return scatter, whole


def digit_perm(axis, stride, radix, offset):
    pairs = []
    for i in range(lax.axis_size(axis)):
        digit = (i // stride) % radix
        pairs.append((i, i + (((digit + offset) % radix) - digit) * stride))
    return pairs


def tree_sum(value, groups):
    scatter, whole_groups = groups
    done = []
    for axis, stride, radix in scatter:
        piece = value.shape[0] // radix
        digit = (lax.axis_index(axis) // stride) % radix
        total = lax.dynamic_slice_in_dim(value, digit * piece, piece, 0)
        for offset in range(1, radix):
            send = lax.dynamic_slice_in_dim(value, ((digit + offset) % radix) * piece, piece, 0)
            total = total + lax.ppermute(send, axis, digit_perm(axis, stride, radix, offset))
        value = total
        done.append((axis, stride, radix, digit))
    for axis, stride, radix in whole_groups:
        digit = (lax.axis_index(axis) // stride) % radix
        arrived = [value] + [
            lax.ppermute(value, axis, digit_perm(axis, stride, radix, offset)) for offset in range(1, radix)
        ]
        stacked = jnp.stack(arrived)
        value = lax.dynamic_index_in_dim(stacked, digit % radix, keepdims=False)
        for source in range(1, radix):
            value = value + lax.dynamic_index_in_dim(stacked, (digit - source) % radix, keepdims=False)
    for axis, stride, radix, digit in reversed(done):
        piece = value.shape[0]
        whole = jnp.zeros((piece * radix,) + value.shape[1:], value.dtype)
        whole = lax.dynamic_update_slice_in_dim(whole, value, digit * piece, 0)
        for offset in range(1, radix):
            got = lax.ppermute(value, axis, digit_perm(axis, stride, radix, offset))
            whole = lax.dynamic_update_slice_in_dim(whole, got, ((digit - offset) % radix) * piece, 0)
        value = whole
    return value

def body(tangents, base_flow):
    highest = lax.Precision.HIGHEST
    slope_one = tendency(add_rim(tangents, 2), base_flow)
    slope_two = tendency(add_rim(tangents + 0.5 * time_step * slope_one, 2), base_flow)
    slope_three = tendency(add_rim(tangents + 0.5 * time_step * slope_two, 2), base_flow)
    slope_four = tendency(add_rim(tangents + time_step * slope_three, 2), base_flow)
    advanced = combine_sections(tangents, slope_one, slope_two, slope_three, slope_four)
    cells = tangents.shape[0] * lax.axis_size("gx") * tangents.shape[1] * lax.axis_size("gy")
    width_vec = advanced.shape[3]
    total_vec = width_vec * lax.axis_size("vec")
    points = lax.all_to_all(advanced, "vec", split_axis=0, concat_axis=3, tiled=True)
    flat_rows = points.reshape(-1, total_vec)
    partial_value = lax.dot_general(
        flat_rows,
        flat_rows,
        (((0,), (0,)), ((), ())),
        precision=highest,
        preferred_element_type=jnp.float32,
    )
    gram_matrix = tree_sum(partial_value, reduce_groups()) / cells
    root = inverse_root(gram_matrix)
    parts = lax.axis_size("vec")
    me = lax.axis_index("vec")
    rows = points.shape[0]
    rotated = jnp.zeros(tangents.shape, tangents.dtype)
    for offset in range(parts):
        target = (me + offset) % parts
        columns = lax.dynamic_slice_in_dim(root, target * width_vec, width_vec, 1)
        turned = jnp.dot(flat_rows, columns, precision=highest, preferred_element_type=jnp.float32)
        turned = turned.reshape(points.shape[:3] + (width_vec,))
        if offset:
            turned = lax.ppermute(turned, "vec", digit_perm("vec", 1, parts, offset))
        source = (me - offset) % parts
        rotated = lax.dynamic_update_slice_in_dim(rotated, turned, source * rows, 0)
    return rotated


def solution(mesh):
    in_specs = (P("gx", "gy", None, "vec"), P("gx", "gy", None))
    out_specs = P("gx", "gy", None, "vec")
    return jax.shard_map(body, mesh=mesh, in_specs=in_specs, out_specs=out_specs, check_vma=False)
```

```python
import jax
import jax.numpy as jnp
from jax import lax
from jax.sharding import PartitionSpec as P

NS_ITERS = 4


time_step = 0.25
viscous = 0.05
spreading_share = 0.05
buoyancy = 1.0


def with_halo(value, sides, width, wrap):
    for axis, dim in sides:
        size, length = (lax.axis_size(axis), value.shape[dim])
        up = [(i, (i + 1) % size) for i in range(size if wrap else size - 1)]
        down = [(j, i) for i, j in up]
        last = lax.slice_in_dim(value, length - width, length, axis=dim)
        leading = lax.slice_in_dim(value, 0, width, axis=dim)
        before = lax.ppermute(last, axis, up)
        after = lax.ppermute(leading, axis, down)
        value = jnp.concatenate([before, value, after], axis=dim)
    return value


def tendency(padded, flow):
    middle_node = padded[2:-2, 2:-2]
    east_two = padded[4:, 2:-2]
    east_one = padded[3:-1, 2:-2]
    west_one = padded[1:-3, 2:-2]
    west_two = padded[:-4, 2:-2]
    north_two = padded[2:-2, 4:]
    north_one = padded[2:-2, 3:-1]
    south_one = padded[2:-2, 1:-3]
    south_two = padded[2:-2, :-4]
    deriv_x = (8.0 * (east_one - west_one) - (east_two - west_two)) / 12.0
    deriv_y = (8.0 * (north_one - south_one) - (north_two - south_two)) / 12.0
    second_derivative_sum = (
        16.0 * (east_one + west_one + north_one + south_one)
        - (east_two + west_two + north_two + south_two)
        - 60.0 * middle_node
    ) / 12.0
    vel_x = flow[:, :, 0][:, :, None, None]
    vel_y = flow[:, :, 1][:, :, None, None]
    thermal_forcing = flow[:, :, 2][:, :, None, None]
    transport_share = -(vel_x * deriv_x + vel_y * deriv_y)
    spread = jnp.array([viscous, spreading_share], jnp.float32)[:, None]
    coupling = jnp.concatenate(
        [buoyancy * deriv_x[:, :, 1:2], thermal_forcing * middle_node[:, :, 0:1]], axis=2
    )
    return transport_share + spread * second_derivative_sum + coupling


def combine_sections(field, slope_one, slope_two, slope_three, slope_four):
    return field + time_step / 6.0 * (slope_one + 2.0 * slope_two + 2.0 * slope_three + slope_four)


def add_rim(field, width):
    wider = with_halo(field, (("gx", 0),), width, True)
    side = with_halo(field, (("gy", 1),), width, False)
    below = jnp.pad(side[:, :width], ((width, width),) + ((0, 0),) * (field.ndim - 1))
    above = jnp.pad(side[:, -width:], ((width, width),) + ((0, 0),) * (field.ndim - 1))
    return jnp.concatenate([below, wider, above], axis=1)


def inverse_root(gram_matrix):
    highest = lax.Precision.HIGH
    scale_norm = jnp.sqrt(jnp.sum(gram_matrix * gram_matrix) + 1e-06)
    identity = jnp.eye(gram_matrix.shape[0], dtype=jnp.float32)
    iterate_y = gram_matrix / scale_norm
    iterate_z = None
    for iteration in range(NS_ITERS):
        if iterate_z is None:
            product = iterate_y
        else:
            product = jnp.dot(iterate_z, iterate_y, precision=highest, preferred_element_type=jnp.float32)
        poly = 1.5 * identity - 0.5 * product
        if iteration + 1 < NS_ITERS:
            iterate_y = jnp.dot(iterate_y, poly, precision=highest, preferred_element_type=jnp.float32)
        if iterate_z is None:
            iterate_z = poly
        else:
            iterate_z = jnp.dot(poly, iterate_z, precision=highest, preferred_element_type=jnp.float32)
    return iterate_z / jnp.sqrt(scale_norm)


def reduce_groups():
    groups = []
    for axis in ("gy", "vec", "gx"):
        size = lax.axis_size(axis)
        assert size & (size - 1) == 0
        stride = 1
        if axis == "gy" and size > 1:
            groups.append((axis, 1, 2))
            stride = 2
        while stride < size:
            radix = 2 if axis == "gx" and stride == 1 and size > 4 else min(4, size // stride)
            groups.append((axis, stride, radix))
            stride *= radix
    scatter = [group for group in groups if group[0] != "gx"]
    whole = [group for group in groups if group[0] == "gx"]
    return scatter, whole


def digit_perm(axis, stride, radix, offset):
    pairs = []
    for i in range(lax.axis_size(axis)):
        digit = (i // stride) % radix
        pairs.append((i, i + (((digit + offset) % radix) - digit) * stride))
    return pairs


def tree_sum(value, groups):
    scatter, whole_groups = groups
    done = []
    for axis, stride, radix in scatter:
        piece = value.shape[0] // radix
        digit = (lax.axis_index(axis) // stride) % radix
        total = lax.dynamic_slice_in_dim(value, digit * piece, piece, 0)
        for offset in range(1, radix):
            send = lax.dynamic_slice_in_dim(value, ((digit + offset) % radix) * piece, piece, 0)
            total = total + lax.ppermute(send, axis, digit_perm(axis, stride, radix, offset))
        value = total
        done.append((axis, stride, radix, digit))
    for axis, stride, radix in whole_groups:
        digit = (lax.axis_index(axis) // stride) % radix
        arrived = [value] + [
            lax.ppermute(value, axis, digit_perm(axis, stride, radix, offset)) for offset in range(1, radix)
        ]
        stacked = jnp.stack(arrived)
        value = lax.dynamic_index_in_dim(stacked, digit % radix, keepdims=False)
        for source in range(1, radix):
            value = value + lax.dynamic_index_in_dim(stacked, (digit - source) % radix, keepdims=False)
    for axis, stride, radix, digit in reversed(done):
        piece = value.shape[0]
        whole = jnp.zeros((piece * radix,) + value.shape[1:], value.dtype)
        whole = lax.dynamic_update_slice_in_dim(whole, value, digit * piece, 0)
        for offset in range(1, radix):
            got = lax.ppermute(value, axis, digit_perm(axis, stride, radix, offset))
            whole = lax.dynamic_update_slice_in_dim(whole, got, ((digit - offset) % radix) * piece, 0)
        value = whole
    return value

def body(tangents, base_flow):
    highest = lax.Precision.HIGHEST
    slope_one = tendency(add_rim(tangents, 2), base_flow)
    slope_two = tendency(add_rim(tangents + 0.5 * time_step * slope_one, 2), base_flow)
    slope_three = tendency(add_rim(tangents + 0.5 * time_step * slope_two, 2), base_flow)
    slope_four = tendency(add_rim(tangents + time_step * slope_three, 2), base_flow)
    advanced = combine_sections(tangents, slope_one, slope_two, slope_three, slope_four)
    cells = tangents.shape[0] * lax.axis_size("gx") * tangents.shape[1] * lax.axis_size("gy")
    width_vec = advanced.shape[3]
    total_vec = width_vec * lax.axis_size("vec")
    points = lax.all_to_all(advanced, "vec", split_axis=0, concat_axis=3, tiled=True)
    flat_rows = points.reshape(-1, total_vec)
    partial_value = lax.dot_general(
        flat_rows,
        flat_rows,
        (((0,), (0,)), ((), ())),
        precision=highest,
        preferred_element_type=jnp.float32,
    )
    gram_matrix = tree_sum(partial_value, reduce_groups()) / cells
    root = inverse_root(gram_matrix)
    parts = lax.axis_size("vec")
    me = lax.axis_index("vec")
    rows = points.shape[0]
    rotated = jnp.zeros(tangents.shape, tangents.dtype)
    for offset in list(range(1, parts)) + [0]:
        target = (me + offset) % parts
        columns = lax.dynamic_slice_in_dim(root, target * width_vec, width_vec, 1)
        turned = jnp.dot(flat_rows, columns, precision=highest, preferred_element_type=jnp.float32)
        turned = turned.reshape(points.shape[:3] + (width_vec,))
        if offset:
            turned = lax.ppermute(turned, "vec", digit_perm("vec", 1, parts, offset))
        source = (me - offset) % parts
        rotated = lax.dynamic_update_slice_in_dim(rotated, turned, source * rows, 0)
    return rotated


def solution(mesh):
    in_specs = (P("gx", "gy", None, "vec"), P("gx", "gy", None))
    out_specs = P("gx", "gy", None, "vec")
    return jax.shard_map(body, mesh=mesh, in_specs=in_specs, out_specs=out_specs, check_vma=False)
```

```python
import jax
import jax.numpy as jnp
from jax import lax
from jax.sharding import PartitionSpec as P

NS_ITERS = 4


time_step = 0.25
viscous = 0.05
spreading_share = 0.05
buoyancy = 1.0


def with_halo(value, sides, width, wrap):
    for axis, dim in sides:
        size, length = (lax.axis_size(axis), value.shape[dim])
        up = [(i, (i + 1) % size) for i in range(size if wrap else size - 1)]
        down = [(j, i) for i, j in up]
        last = lax.slice_in_dim(value, length - width, length, axis=dim)
        leading = lax.slice_in_dim(value, 0, width, axis=dim)
        before = lax.ppermute(last, axis, up)
        after = lax.ppermute(leading, axis, down)
        value = jnp.concatenate([before, value, after], axis=dim)
    return value


def tendency(padded, flow):
    middle_node = padded[2:-2, 2:-2]
    east_two = padded[4:, 2:-2]
    east_one = padded[3:-1, 2:-2]
    west_one = padded[1:-3, 2:-2]
    west_two = padded[:-4, 2:-2]
    north_two = padded[2:-2, 4:]
    north_one = padded[2:-2, 3:-1]
    south_one = padded[2:-2, 1:-3]
    south_two = padded[2:-2, :-4]
    deriv_x = (8.0 * (east_one - west_one) - (east_two - west_two)) / 12.0
    deriv_y = (8.0 * (north_one - south_one) - (north_two - south_two)) / 12.0
    second_derivative_sum = (
        16.0 * (east_one + west_one + north_one + south_one)
        - (east_two + west_two + north_two + south_two)
        - 60.0 * middle_node
    ) / 12.0
    vel_x = flow[:, :, 0][:, :, None, None]
    vel_y = flow[:, :, 1][:, :, None, None]
    thermal_forcing = flow[:, :, 2][:, :, None, None]
    transport_share = -(vel_x * deriv_x + vel_y * deriv_y)
    spread = jnp.array([viscous, spreading_share], jnp.float32)[:, None]
    coupling = jnp.concatenate(
        [buoyancy * deriv_x[:, :, 1:2], thermal_forcing * middle_node[:, :, 0:1]], axis=2
    )
    return transport_share + spread * second_derivative_sum + coupling


def combine_sections(field, slope_one, slope_two, slope_three, slope_four):
    return field + time_step / 6.0 * (slope_one + 2.0 * slope_two + 2.0 * slope_three + slope_four)


def add_rim(field, width):
    wider = with_halo(field, (("gx", 0),), width, True)
    side = with_halo(field, (("gy", 1),), width, False)
    below = jnp.pad(side[:, :width], ((width, width),) + ((0, 0),) * (field.ndim - 1))
    above = jnp.pad(side[:, -width:], ((width, width),) + ((0, 0),) * (field.ndim - 1))
    return jnp.concatenate([below, wider, above], axis=1)


def inverse_root(gram_matrix):
    highest = lax.Precision.HIGH
    scale_norm = jnp.sqrt(jnp.sum(gram_matrix * gram_matrix) + 1e-06)
    identity = jnp.eye(gram_matrix.shape[0], dtype=jnp.float32)
    iterate_y = gram_matrix / scale_norm
    iterate_z = None
    for iteration in range(NS_ITERS):
        if iterate_z is None:
            product = iterate_y
        else:
            product = jnp.dot(iterate_z, iterate_y, precision=highest, preferred_element_type=jnp.float32)
        poly = 1.5 * identity - 0.5 * product
        if iteration + 1 < NS_ITERS:
            iterate_y = jnp.dot(iterate_y, poly, precision=highest, preferred_element_type=jnp.float32)
        if iterate_z is None:
            iterate_z = poly
        else:
            iterate_z = jnp.dot(poly, iterate_z, precision=highest, preferred_element_type=jnp.float32)
    return iterate_z / jnp.sqrt(scale_norm)


def reduce_groups():
    groups = []
    for axis in ("gy", "vec", "gx"):
        size = lax.axis_size(axis)
        assert size & (size - 1) == 0
        stride = 1
        if axis == "gy" and size > 1:
            groups.append((axis, 1, 2))
            stride = 2
        while stride < size:
            radix = 2 if axis == "gx" and stride == 1 and size > 4 else min(4, size // stride)
            groups.append((axis, stride, radix))
            stride *= radix
    scatter = [group for group in groups if group[0] != "gx"]
    whole = [group for group in groups if group[0] == "gx"]
    return scatter, whole


def digit_perm(axis, stride, radix, offset):
    pairs = []
    for i in range(lax.axis_size(axis)):
        digit = (i // stride) % radix
        pairs.append((i, i + (((digit + offset) % radix) - digit) * stride))
    return pairs


def tree_sum(value, groups):
    scatter, whole_groups = groups
    done = []
    for axis, stride, radix in scatter:
        piece = value.shape[0] // radix
        digit = (lax.axis_index(axis) // stride) % radix
        total = lax.dynamic_slice_in_dim(value, digit * piece, piece, 0)
        for offset in range(1, radix):
            send = lax.dynamic_slice_in_dim(value, ((digit + offset) % radix) * piece, piece, 0)
            total = total + lax.ppermute(send, axis, digit_perm(axis, stride, radix, offset))
        value = total
        done.append((axis, stride, radix, digit))
    for axis, stride, radix in whole_groups:
        digit = (lax.axis_index(axis) // stride) % radix
        arrived = [value] + [
            lax.ppermute(value, axis, digit_perm(axis, stride, radix, offset)) for offset in range(1, radix)
        ]
        stacked = jnp.stack(arrived)
        value = lax.dynamic_index_in_dim(stacked, digit % radix, keepdims=False)
        for source in range(1, radix):
            value = value + lax.dynamic_index_in_dim(stacked, (digit - source) % radix, keepdims=False)
    for axis, stride, radix, digit in reversed(done):
        piece = value.shape[0]
        whole = jnp.zeros((piece * radix,) + value.shape[1:], value.dtype)
        whole = lax.dynamic_update_slice_in_dim(whole, value, digit * piece, 0)
        for offset in range(1, radix):
            got = lax.ppermute(value, axis, digit_perm(axis, stride, radix, offset))
            whole = lax.dynamic_update_slice_in_dim(whole, got, ((digit - offset) % radix) * piece, 0)
        value = whole
    return value

def body(tangents, base_flow):
    highest = lax.Precision.HIGH
    slope_one = tendency(add_rim(tangents, 2), base_flow)
    slope_two = tendency(add_rim(tangents + 0.5 * time_step * slope_one, 2), base_flow)
    slope_three = tendency(add_rim(tangents + 0.5 * time_step * slope_two, 2), base_flow)
    slope_four = tendency(add_rim(tangents + time_step * slope_three, 2), base_flow)
    advanced = combine_sections(tangents, slope_one, slope_two, slope_three, slope_four)
    cells = tangents.shape[0] * lax.axis_size("gx") * tangents.shape[1] * lax.axis_size("gy")
    width_vec = advanced.shape[3]
    total_vec = width_vec * lax.axis_size("vec")
    points = lax.all_to_all(advanced, "vec", split_axis=0, concat_axis=3, tiled=True)
    flat_rows = points.reshape(-1, total_vec)
    partial_value = lax.dot_general(
        flat_rows,
        flat_rows,
        (((0,), (0,)), ((), ())),
        precision=highest,
        preferred_element_type=jnp.float32,
    )
    gram_matrix = tree_sum(partial_value, reduce_groups()) / cells
    root = inverse_root(gram_matrix)
    parts = lax.axis_size("vec")
    me = lax.axis_index("vec")
    rows = points.shape[0]
    rotated = jnp.zeros(tangents.shape, tangents.dtype)
    for offset in range(parts):
        target = (me + offset) % parts
        columns = lax.dynamic_slice_in_dim(root, target * width_vec, width_vec, 1)
        turned = jnp.dot(flat_rows, columns, precision=highest, preferred_element_type=jnp.float32)
        turned = turned.reshape(points.shape[:3] + (width_vec,))
        if offset:
            turned = lax.ppermute(turned, "vec", digit_perm("vec", 1, parts, offset))
        source = (me - offset) % parts
        rotated = lax.dynamic_update_slice_in_dim(rotated, turned, source * rows, 0)
    return rotated


def solution(mesh):
    in_specs = (P("gx", "gy", None, "vec"), P("gx", "gy", None))
    out_specs = P("gx", "gy", None, "vec")
    return jax.shard_map(body, mesh=mesh, in_specs=in_specs, out_specs=out_specs, check_vma=False)
```
